768 devices in a mesh: row: 32 (over x, y_lo, core), col: 24 (over y_hi, z).
Axes of the slice: x: 4, y: 8 (y_hi: 2, y_lo: 4; y = y_hi * 4 + y_lo), z: 12, core: 2. Of those that a mesh axis runs over, the one named last changes fastest.
Arguments:
- inputs: bfloat16 [1536, 8192], P(None, 'row'), may hold values from -6 to 6
- gate_weight: bfloat16 [8192, 27648], P('row', 'col'), may hold values from -0.0625 to 0.0625
- up_weight: bfloat16 [8192, 27648], P('row', 'col'), may hold values from -0.0625 to 0.0625
- gate_pre: bfloat16 [1536, 27648], P('row', 'col'), may hold values from -6 to 6
- up_pre: bfloat16 [1536, 27648], P('row', 'col'), may hold values from -6 to 6
- grad_act: bfloat16 [1536, 27648], P('row', 'col'), may hold values from -1.1953125 to 1.1953125
Outputs:
- grad_input: bfloat16 [1536, 8192], P('col', 'row')
- grad_gate_weight: bfloat16 [8192, 27648], P('row', 'col')
- grad_up_weight: bfloat16 [8192, 27648], P('row', 'col')
The draws below stay inside these ranges and needn't reach their ends.
All inputs are finite; a program needn't handle non-finite values.
Results may differ from the reference program's by a relative error of at most 0.0049.
Values may be sent and summed in bfloat16 or wider, within the bound.
No kernel may reach another device: no remote copies, remote signals or barrier semaphores. Data moves between devices by JAX's collectives and lax.ppermute only.
A program may use at most 32 MiB of HBM per device.

```python
import jax
import jax.numpy as jnp

D = 8192
FF = 27648
TOKENS = 1536


def block_scale(rng, shape, shards, smallest, high):
    gain = 1.0
    for dim, blocks in shards:
        draws = jax.random.uniform(jax.random.fold_in(jax.random.fold_in(rng, 6), dim), (blocks,), jnp.float32, smallest / len(shards), high / len(shards))
        gain = gain * jnp.repeat(jnp.exp(draws), shape[dim] // blocks).reshape((-1,) + (1,) * (len(shape) - 1 - dim))
    return gain


def normal_values(rng, dims, width, most, cuts=(), kind=jnp.bfloat16):
    result = jax.random.normal(rng, dims, jnp.float32) * width
    if len(cuts) > 0:
        result = block_scale(rng, dims, cuts, -0.22, 0.18) * result
    return jnp.clip(result, min=-most, max=most).astype(kind)


def setup_inputs(seed: int = 0) -> dict:
    key_of = jax.random.split(jax.random.key(seed), 7)
    inputs = normal_values(key_of[0], (TOKENS, D), 1.0, 6.0, ((1, 32),))
    gate_weight = normal_values(key_of[1], (D, FF), D ** -0.5, 0.0625, ((0, 32), (1, 24)))
    up_weight = normal_values(key_of[2], (D, FF), D ** -0.5, 0.0625, ((0, 32), (1, 24)))
    gate_pre = normal_values(key_of[3], (TOKENS, FF), 1.0, 6.0, ((0, 32), (1, 24)))
    up_pre = normal_values(key_of[4], (TOKENS, FF), 1.0, 6.0, ((0, 32), (1, 24)))
    grad_act = normal_values(key_of[5], (TOKENS, FF), 0.2, 1.1953125, ((0, 32), (1, 24)))
    return dict(inputs=inputs, gate_weight=gate_weight, up_weight=up_weight, gate_pre=gate_pre, up_pre=up_pre, grad_act=grad_act)


def reference(inputs, gate_weight, up_weight, gate_pre, up_pre, grad_act):
    gate32 = gate_pre.astype(jnp.float32)
    up32 = up_pre.astype(jnp.float32)
    grad32 = grad_act.astype(jnp.float32)
    sig = jax.nn.sigmoid(gate32)
    grad_gate = (grad32 * up32 * sig * (1.0 + gate32 * (1.0 - sig))).astype(jnp.bfloat16)
    grad_up = (grad32 * gate32 * sig).astype(jnp.bfloat16)
    grad_gate_weight = jnp.dot(inputs.T, grad_gate, preferred_element_type=jnp.float32).astype(jnp.bfloat16)
    grad_up_weight = jnp.dot(inputs.T, grad_up, preferred_element_type=jnp.float32).astype(jnp.bfloat16)
    partial_gate = jnp.dot(grad_gate, gate_weight.T, preferred_element_type=jnp.float32)
    partial_up = jnp.dot(grad_up, up_weight.T, preferred_element_type=jnp.float32)
    grad_input = (partial_gate + partial_up).astype(jnp.bfloat16)
    return grad_input, grad_gate_weight, grad_up_weight
```

```python
import jax
import jax.numpy as jnp
from jax import lax
from jax.sharding import PartitionSpec as P


def contract_rows(left, right):
    return lax.dot_general(
        left, right, (((0,), (0,)), ((), ())), preferred_element_type=jnp.float32
    )


def contract_cols(left, right):
    return lax.dot_general(
        left, right, (((1,), (1,)), ((), ())), preferred_element_type=jnp.float32
    )


def reduce_input(partial_input):
    parts = lax.psum(1, "col")
    rows, width = partial_input.shape
    pieces = partial_input.reshape(parts, rows // parts, width)
    pieces = lax.all_to_all(pieces, "col", 0, 0, tiled=False)
    return pieces.sum(0).astype(jnp.bfloat16)


def on_device(inputs, gate_weight, up_weight, gate_pre, up_pre, grad_act):
    gate32 = gate_pre.astype(jnp.float32)
    up32 = up_pre.astype(jnp.float32)
    grad32 = grad_act.astype(jnp.float32)
    sig = jax.nn.sigmoid(gate32)
    grad_gate = (grad32 * up32 * sig * (1.0 + gate32 * (1.0 - sig))).astype(jnp.bfloat16)
    grad_up = (grad32 * gate32 * sig).astype(jnp.bfloat16)
    width = grad_gate.shape[1]
    both = lax.all_gather(jnp.concatenate([grad_gate, grad_up], 1), "row", axis=0, tiled=True)
    piece_gate, piece_up = both[:, :width], both[:, width:]
    acc_gate = contract_rows(inputs, piece_gate)
    acc_up = contract_rows(inputs, piece_up)
    part = contract_cols(piece_gate, gate_weight) + contract_cols(piece_up, up_weight)
    acc_gate, acc_up, partial_input = (acc_gate, acc_up, part)
    grad_input = reduce_input(partial_input)
    return (grad_input, acc_gate.astype(jnp.bfloat16), acc_up.astype(jnp.bfloat16))


def solution(mesh):
    return jax.shard_map(
        on_device,
        mesh=mesh,
        in_specs=(
            P(None, "row"),
            P("row", "col"),
            P("row", "col"),
            P("row", "col"),
            P("row", "col"),
            P("row", "col"),
        ),
        out_specs=(P("col", "row"), P("row", "col"), P("row", "col")),
        check_vma=False,
    )
```

```python
import jax
import jax.numpy as jnp
from jax import lax
from jax.sharding import PartitionSpec as P

PERIOD = 16
CHUNKS = 2


def contract_rows(left, right):
    return lax.dot_general(
        left, right, (((0,), (0,)), ((), ())), preferred_element_type=jnp.float32
    )


def contract_cols(left, right):
    return lax.dot_general(
        left, right, (((1,), (1,)), ((), ())), preferred_element_type=jnp.float32
    )


def take_chunk(rows, index):
    size = PERIOD // CHUNKS
    grouped = rows.reshape(rows.shape[0] // PERIOD, PERIOD, rows.shape[1])
    return grouped[:, index * size:(index + 1) * size].reshape(-1, rows.shape[1])


def reduce_input(partial_input):
    parts = lax.psum(1, "col")
    rows, width = partial_input.shape
    pieces = partial_input.reshape(parts, rows // parts, width)
    pieces = lax.all_to_all(pieces, "col", 0, 0, tiled=False)
    return pieces.sum(0)


def on_device(inputs, gate_weight, up_weight, gate_pre, up_pre, grad_act):
    gate32 = gate_pre.astype(jnp.float32)
    up32 = up_pre.astype(jnp.float32)
    grad32 = grad_act.astype(jnp.float32)
    sig = jax.nn.sigmoid(gate32)
    grad_gate = (grad32 * up32 * sig * (1.0 + gate32 * (1.0 - sig))).astype(jnp.bfloat16)
    grad_up = (grad32 * gate32 * sig).astype(jnp.bfloat16)
    width = grad_gate.shape[1]
    both = jnp.concatenate([grad_gate, grad_up], 1)
    acc_gate = None
    acc_up = None
    outs = []
    for index in range(CHUNKS):
        piece = lax.all_gather(take_chunk(both, index), "row", axis=0, tiled=True)
        piece_gate, piece_up = piece[:, :width], piece[:, width:]
        rows = take_chunk(inputs, index)
        step_gate = contract_rows(rows, piece_gate)
        step_up = contract_rows(rows, piece_up)
        acc_gate = step_gate if acc_gate is None else acc_gate + step_gate
        acc_up = step_up if acc_up is None else acc_up + step_up
        part = contract_cols(piece_gate, gate_weight) + contract_cols(piece_up, up_weight)
        out = reduce_input(part)
        outs.append(out.reshape(-1, PERIOD // CHUNKS, out.shape[1]))
    grad_input = jnp.stack(outs, 1).reshape(-1, outs[0].shape[2]).astype(jnp.bfloat16)
    return (grad_input, acc_gate.astype(jnp.bfloat16), acc_up.astype(jnp.bfloat16))


def solution(mesh):
    return jax.shard_map(
        on_device,
        mesh=mesh,
        in_specs=(
            P(None, "row"),
            P("row", "col"),
            P("row", "col"),
            P("row", "col"),
            P("row", "col"),
            P("row", "col"),
        ),
        out_specs=(P("col", "row"), P("row", "col"), P("row", "col")),
        check_vma=False,
    )
```

```python
import jax
import jax.numpy as jnp
from jax import lax
from jax.sharding import PartitionSpec as P


def contract_rows(left, right):
    return lax.dot_general(
        left, right, (((0,), (0,)), ((), ())), preferred_element_type=jnp.float32
    )


def contract_cols(left, right):
    return lax.dot_general(
        left, right, (((1,), (1,)), ((), ())), preferred_element_type=jnp.float32
    )


def reduce_input(partial_input):
    parts = lax.psum(1, "col")
    rows, width = partial_input.shape
    pieces = partial_input.reshape(parts, rows // parts, width)
    pieces = lax.all_to_all(pieces, "col", 0, 0, tiled=False)
    return pieces.sum(0).astype(jnp.bfloat16)


def on_device(inputs, gate_weight, up_weight, gate_pre, up_pre, grad_act):
    gate32 = gate_pre.astype(jnp.float32)
    up32 = up_pre.astype(jnp.float32)
    grad32 = grad_act.astype(jnp.float32)
    sig = jax.nn.sigmoid(gate32)
    grad_gate = (grad32 * up32 * sig * (1.0 + gate32 * (1.0 - sig))).astype(jnp.bfloat16)
    grad_up = (grad32 * gate32 * sig).astype(jnp.bfloat16)
    width = grad_gate.shape[1]
    both = lax.all_gather(jnp.concatenate([grad_gate, grad_up], 1), "row", axis=0, tiled=True)
    acc = contract_rows(inputs, both)
    acc_gate, acc_up = acc[:, :width], acc[:, width:]
    weights = jnp.concatenate([gate_weight, up_weight], 1)
    partial_input = contract_cols(both, weights)
    grad_input = reduce_input(partial_input)
    return (grad_input, acc_gate.astype(jnp.bfloat16), acc_up.astype(jnp.bfloat16))


def solution(mesh):
    return jax.shard_map(
        on_device,
        mesh=mesh,
        in_specs=(
            P(None, "row"),
            P("row", "col"),
            P("row", "col"),
            P("row", "col"),
            P("row", "col"),
            P("row", "col"),
        ),
        out_specs=(P("col", "row"), P("row", "col"), P("row", "col")),
        check_vma=False,
    )
```

```python
import jax
import jax.numpy as jnp
from jax import lax
from jax.experimental import pallas as pl
from jax.sharding import PartitionSpec as P

TILE_ROWS = 768


def contract_rows(left, right):
    return lax.dot_general(
        left, right, (((0,), (0,)), ((), ())), preferred_element_type=jnp.float32
    )


def contract_cols(left, right):
    return lax.dot_general(
        left, right, (((1,), (1,)), ((), ())), preferred_element_type=jnp.float32
    )


def input_kernel(both_ref, gate_ref, up_ref, out_ref):
    width = gate_ref.shape[1]
    dims = (((1,), (1,)), ((), ()))
    out_ref[...] = lax.dot_general(
        both_ref[:, :width], gate_ref[...], dims, preferred_element_type=jnp.float32
    ) + lax.dot_general(
        both_ref[:, width:], up_ref[...], dims, preferred_element_type=jnp.float32
    )


def partial_input_of(both, gate_weight, up_weight):
    rows, width = both.shape
    features = gate_weight.shape[0]
    tile = TILE_ROWS if rows % TILE_ROWS == 0 else rows
    return pl.pallas_call(
        input_kernel,
        grid=(rows // tile,),
        in_specs=[
            pl.BlockSpec((tile, width), lambda i: (i, 0)),
            pl.BlockSpec(gate_weight.shape, lambda i: (0, 0)),
            pl.BlockSpec(up_weight.shape, lambda i: (0, 0)),
        ],
        out_specs=pl.BlockSpec((tile, features), lambda i: (i, 0)),
        out_shape=jax.ShapeDtypeStruct((rows, features), jnp.float32),
        cost_estimate=pl.CostEstimate(
            flops=2 * rows * width * features,
            bytes_accessed=2 * (rows * width + 2 * features * gate_weight.shape[1]) + 4 * rows * features,
            transcendentals=0,
        ),
    )(both, gate_weight, up_weight)


def reduce_input(partial_input):
    parts = lax.psum(1, "col")
    rows, width = partial_input.shape
    pieces = partial_input.reshape(parts, rows // parts, width)
    pieces = lax.all_to_all(pieces, "col", 0, 0, tiled=False)
    return pieces.sum(0).astype(jnp.bfloat16)


def on_device(inputs, gate_weight, up_weight, gate_pre, up_pre, grad_act):
    gate32 = gate_pre.astype(jnp.float32)
    up32 = up_pre.astype(jnp.float32)
    grad32 = grad_act.astype(jnp.float32)
    sig = jax.nn.sigmoid(gate32)
    grad_gate = (grad32 * up32 * sig * (1.0 + gate32 * (1.0 - sig))).astype(jnp.bfloat16)
    grad_up = (grad32 * gate32 * sig).astype(jnp.bfloat16)
    width = grad_gate.shape[1]
    both = lax.all_gather(jnp.concatenate([grad_gate, grad_up], 1), "row", axis=0, tiled=True)
    acc = contract_rows(inputs, both)
    acc_gate, acc_up = acc[:, :width], acc[:, width:]
    partial_input = partial_input_of(both, gate_weight, up_weight)
    grad_input = reduce_input(partial_input)
    return (grad_input, acc_gate.astype(jnp.bfloat16), acc_up.astype(jnp.bfloat16))


def solution(mesh):
    return jax.shard_map(
        on_device,
        mesh=mesh,
        in_specs=(
            P(None, "row"),
            P("row", "col"),
            P("row", "col"),
            P("row", "col"),
            P("row", "col"),
            P("row", "col"),
        ),
        out_specs=(P("col", "row"), P("row", "col"), P("row", "col")),
        check_vma=False,
    )
```

```python
import jax
import jax.numpy as jnp
from jax import lax
from jax.experimental import pallas as pl
from jax.sharding import PartitionSpec as P

TILE_ROWS = 768


def contract_rows(left, right):
    return lax.dot_general(
        left, right, (((0,), (0,)), ((), ())), preferred_element_type=jnp.float32
    )


def contract_cols(left, right):
    return lax.dot_general(
        left, right, (((1,), (1,)), ((), ())), preferred_element_type=jnp.float32
    )


def input_kernel(both_ref, gate_ref, up_ref, out_ref):
    width = gate_ref.shape[1]
    dims = (((1,), (1,)), ((), ()))
    out_ref[...] = lax.dot_general(
        both_ref[:, :width], gate_ref[...], dims, preferred_element_type=jnp.float32
    ) + lax.dot_general(
        both_ref[:, width:], up_ref[...], dims, preferred_element_type=jnp.float32
    )


def partial_input_of(both, gate_weight, up_weight):
    rows, width = both.shape
    features = gate_weight.shape[0]
    tile = TILE_ROWS if rows % TILE_ROWS == 0 else rows
    return pl.pallas_call(
        input_kernel,
        grid=(rows // tile,),
        in_specs=[
            pl.BlockSpec((tile, width), lambda i: (i, 0)),
            pl.BlockSpec(gate_weight.shape, lambda i: (0, 0)),
            pl.BlockSpec(up_weight.shape, lambda i: (0, 0)),
        ],
        out_specs=pl.BlockSpec((tile, features), lambda i: (i, 0)),
        out_shape=jax.ShapeDtypeStruct((rows, features), jnp.float32),
        cost_estimate=pl.CostEstimate(
            flops=2 * rows * width * features,
            bytes_accessed=2 * (rows * width + 2 * features * gate_weight.shape[1]) + 4 * rows * features,
            transcendentals=0,
        ),
    )(both, gate_weight, up_weight)


def reduce_input(partial_input):
    parts = lax.psum(1, "col")
    rows, width = partial_input.shape
    pieces = partial_input.reshape(parts, rows // parts, width)
    pieces = lax.all_to_all(pieces, "col", 0, 0, tiled=False)
    return pieces.sum(0).astype(jnp.bfloat16)


def on_device(inputs, gate_weight, up_weight, gate_pre, up_pre, grad_act):
    width = gate_pre.shape[1]
    gate32 = jnp.concatenate([gate_pre, gate_pre], 1).astype(jnp.float32)
    up32 = jnp.concatenate([up_pre, up_pre], 1).astype(jnp.float32)
    grad32 = jnp.concatenate([grad_act, grad_act], 1).astype(jnp.float32)
    sig = jax.nn.sigmoid(gate32)
    is_gate = lax.broadcasted_iota(jnp.int32, gate32.shape, 1) < width
    grad_both = jnp.where(
        is_gate, grad32 * up32 * sig * (1.0 + gate32 * (1.0 - sig)), grad32 * gate32 * sig
    ).astype(jnp.bfloat16)
    both = lax.all_gather(grad_both, "row", axis=0, tiled=True)
    acc = contract_rows(inputs, both)
    acc_gate, acc_up = acc[:, :width], acc[:, width:]
    partial_input = partial_input_of(both, gate_weight, up_weight)
    grad_input = reduce_input(partial_input)
    return (grad_input, acc_gate.astype(jnp.bfloat16), acc_up.astype(jnp.bfloat16))


def solution(mesh):
    return jax.shard_map(
        on_device,
        mesh=mesh,
        in_specs=(
            P(None, "row"),
            P("row", "col"),
            P("row", "col"),
            P("row", "col"),
            P("row", "col"),
            P("row", "col"),
        ),
        out_specs=(P("col", "row"), P("row", "col"), P("row", "col")),
        check_vma=False,
    )
```

```python
import jax
import jax.numpy as jnp
from jax import lax
from jax.experimental import pallas as pl
from jax.experimental.pallas import tpu as pltpu
from jax.sharding import PartitionSpec as P

TILE_ROWS = 768


def contract_rows(left, right):
    return lax.dot_general(
        left, right, (((0,), (0,)), ((), ())), preferred_element_type=jnp.float32
    )


def contract_cols(left, right):
    return lax.dot_general(
        left, right, (((1,), (1,)), ((), ())), preferred_element_type=jnp.float32
    )


def grads_kernel(gate_ref, up_ref, grad_ref, out_ref):
    width = gate_ref.shape[1]
    gate32 = gate_ref[...].astype(jnp.float32)
    up32 = up_ref[...].astype(jnp.float32)
    grad32 = grad_ref[...].astype(jnp.float32)
    sig = jax.nn.sigmoid(gate32)
    out_ref[:, :width] = (grad32 * up32 * sig * (1.0 + gate32 * (1.0 - sig))).astype(out_ref.dtype)
    out_ref[:, width:] = (grad32 * gate32 * sig).astype(out_ref.dtype)


def grads_of(gate_pre, up_pre, grad_act):
    rows, width = gate_pre.shape
    return pl.pallas_call(
        grads_kernel,
        in_specs=[pl.BlockSpec(memory_space=pltpu.VMEM)] * 3,
        out_specs=pl.BlockSpec(memory_space=pltpu.VMEM),
        out_shape=jax.ShapeDtypeStruct((rows, 2 * width), jnp.bfloat16),
        cost_estimate=pl.CostEstimate(
            flops=12 * rows * width, bytes_accessed=10 * rows * width, transcendentals=rows * width
        ),
    )(gate_pre, up_pre, grad_act)


def input_kernel(both_ref, gate_ref, up_ref, out_ref):
    width = gate_ref.shape[1]
    dims = (((1,), (1,)), ((), ()))
    out_ref[...] = lax.dot_general(
        both_ref[:, :width], gate_ref[...], dims, preferred_element_type=jnp.float32
    ) + lax.dot_general(
        both_ref[:, width:], up_ref[...], dims, preferred_element_type=jnp.float32
    )


def partial_input_of(both, gate_weight, up_weight):
    rows, width = both.shape
    features = gate_weight.shape[0]
    tile = TILE_ROWS if rows % TILE_ROWS == 0 else rows
    return pl.pallas_call(
        input_kernel,
        grid=(rows // tile,),
        in_specs=[
            pl.BlockSpec((tile, width), lambda i: (i, 0)),
            pl.BlockSpec(gate_weight.shape, lambda i: (0, 0)),
            pl.BlockSpec(up_weight.shape, lambda i: (0, 0)),
        ],
        out_specs=pl.BlockSpec((tile, features), lambda i: (i, 0)),
        out_shape=jax.ShapeDtypeStruct((rows, features), jnp.float32),
        cost_estimate=pl.CostEstimate(
            flops=2 * rows * width * features,
            bytes_accessed=2 * (rows * width + 2 * features * gate_weight.shape[1]) + 4 * rows * features,
            transcendentals=0,
        ),
    )(both, gate_weight, up_weight)


def reduce_input(partial_input):
    parts = lax.psum(1, "col")
    rows, width = partial_input.shape
    pieces = partial_input.reshape(parts, rows // parts, width)
    pieces = lax.all_to_all(pieces, "col", 0, 0, tiled=False)
    return pieces.sum(0).astype(jnp.bfloat16)


def on_device(inputs, gate_weight, up_weight, gate_pre, up_pre, grad_act):
    width = gate_pre.shape[1]
    both = lax.all_gather(grads_of(gate_pre, up_pre, grad_act), "row", axis=0, tiled=True)
    acc = contract_rows(inputs, both)
    acc_gate, acc_up = acc[:, :width], acc[:, width:]
    partial_input = partial_input_of(both, gate_weight, up_weight)
    grad_input = reduce_input(partial_input)
    return (grad_input, acc_gate.astype(jnp.bfloat16), acc_up.astype(jnp.bfloat16))


def solution(mesh):
    return jax.shard_map(
        on_device,
        mesh=mesh,
        in_specs=(
            P(None, "row"),
            P("row", "col"),
            P("row", "col"),
            P("row", "col"),
            P("row", "col"),
            P("row", "col"),
        ),
        out_specs=(P("col", "row"), P("row", "col"), P("row", "col")),
        check_vma=False,
    )
```
